512 devices in a mesh: lon: 64 (over z, y), lat: 4 (over x_hi, core), mem: 2 (over x_lo).
Axes of the slice: x: 4 (x_hi: 2, x_lo: 2; x = x_hi * 2 + x_lo), y: 8, z: 8, core: 2. Of those that a mesh axis runs over, the one named last changes fastest.
Arguments:
- height: float32 [16, 2048, 1024], P('mem', 'lon', 'lat'), may hold values from -6 to 6
- east: float32 [16, 2048, 1024], P('mem', 'lon', 'lat'), may hold values from -3 to 3
- north: float32 [16, 2048, 1024], P('mem', 'lon', 'lat'), may hold values from -3 to 3
- depth: float32 [2048, 1024], P('lon', 'lat'), may hold values from 0.5 to 2
- coriolis: float32 [2048, 1024], P('lon', 'lat'), may hold values from -0.5 to 0.5
- weight_table: float32 [4], replicated, may hold values from 0.2 to 5
- member_index: int32 [16], replicated, may hold values from 0 to 3
- level_table: float32 [16], replicated, may hold values from -4 to 4
- threshold_index: int32 [16], replicated, may hold values from 0 to 15, each once
Outputs:
- heights: float32 [16, 2048, 1024], P('mem', 'lon', 'lat')
- mixture_cdf: float32 [16, 2048, 1024], P('mem', 'lon', 'lat')
The draws below stay inside these ranges and needn't reach their ends.
Inputs may be any that keep to these rules, and one draw needn't show every extreme that they name: `threshold_index`: each threshold names a different level.
All inputs are finite; a program needn't handle non-finite values.
Results may differ from the reference program's by a relative error of at most 0.000024.
Values sent between devices are 32-bit elements; how exact they have to be, the bound alone decides.
No kernel may reach another device: no remote copies, remote signals or barrier semaphores. Data moves between devices by JAX's collectives and lax.ppermute only.
A program may use at most 64 MiB of HBM per device.

```python
import math
import jax
import jax.numpy as jnp
from jax import lax

MEMBERS = 16
ITERS = 8
NTHR = 16
NWEIGHT = 4
NLON = 2048
NLAT = 1024


def set_ends(array, own_key, smallest, top_value):
    index_at = [jax.random.randint(jax.random.fold_in(own_key, axis), (), 0, length) for axis, length in enumerate(array.shape)]
    main_axis = array.shape.index(max(array.shape))
    next_to = index_at[:main_axis] + [(index_at[main_axis] + 1) % array.shape[main_axis]] + index_at[main_axis + 1:]
    return array.at[tuple(index_at)].set(smallest).at[tuple(next_to)].set(top_value)


def block_levels(rng, shape, pieces, least, high):
    def one(dim, blocks):
        steps = jax.random.uniform(jax.random.fold_in(jax.random.fold_in(rng, 6), dim), (blocks,), jnp.float32, least / len(pieces), high / len(pieces))
        return jnp.repeat(jnp.exp(steps), shape[dim] // blocks).reshape((-1,) + (1,) * (len(shape) - dim - 1))

    gain = one(*pieces[0])
    for cut in pieces[1:]:
        gain = gain * one(*cut)
    return gain


def normal_values(rng, dims, deviation, most, pieces=(), kind=jnp.bfloat16):
    result = deviation * jax.random.normal(rng, dims, jnp.float32)
    if pieces:
        result = result * block_levels(rng, dims, pieces, -0.22, 0.18)
    return jnp.clip(result, -most, most).astype(kind)


def setup_inputs(seed: int = 0) -> dict:
    seeds = jax.random.split(jax.random.key(seed), 10)
    return {
        "height": normal_values(seeds[0], (MEMBERS, NLON, NLAT), 1.0, 6.0, ((0, 2), (1, 64), (2, 4)), jnp.float32),
        "east": normal_values(seeds[1], (MEMBERS, NLON, NLAT), 0.5, 3.0, ((0, 2), (1, 64), (2, 4)), jnp.float32),
        "north": normal_values(seeds[2], (MEMBERS, NLON, NLAT), 0.5, 3.0, ((0, 2), (1, 64), (2, 4)), jnp.float32),
        "depth": jnp.clip(0.5 + 1.5 * jax.random.uniform(seeds[3], (NLON, NLAT), jnp.float32) ** block_levels(seeds[3], (NLON, NLAT), ((0, 64), (1, 4)), -0.2, 0.2), 0.5, 2.0),
        "coriolis": jnp.clip(jax.random.uniform(seeds[4], (NLON, NLAT), jnp.float32, -0.5, 0.5) * block_levels(seeds[4], (NLON, NLAT), ((0, 64), (1, 4)), -0.4, 0.0), -0.5, 0.5),
        "weight_table": jnp.clip(jnp.exp(jax.random.uniform(seeds[5], (NWEIGHT,), jnp.float32, math.log(0.2), math.log(5.0))), 0.2, 5.0),
        "member_index": set_ends(jax.random.randint(seeds[6], (MEMBERS,), 0, NWEIGHT), jax.random.fold_in(seeds[6], 1), 0, NWEIGHT - 1).astype(jnp.int32),
        "level_table": normal_values(seeds[7], (NTHR,), 1.5, 4.0, (), jnp.float32),
        "threshold_index": jax.random.permutation(seeds[8], NTHR).astype(jnp.int32),
    }


courant_half = 0.45
kernel_scale = 1.0 / (0.5 * 1.4142135623730951)


def diff_lon(field):
    return jnp.roll(field, -1, axis=1) - jnp.roll(field, 1, axis=1)


def diff_lat(field):
    padded = jnp.pad(field, ((0, 0), (0, 0), (1, 1)))
    return padded[:, :, 2:] - padded[:, :, :-2]


def reference(height, east, north, depth, coriolis, weight_table, member_index, level_table, threshold_index):
    for step in range(ITERS):
        flux_east = depth * east
        flux_north = depth * north
        height = height - courant_half * (diff_lon(flux_east) + diff_lat(flux_north))
        east = east + coriolis * north - courant_half * diff_lon(height)
        north = north - coriolis * east - courant_half * diff_lat(height)
    picked = weight_table[member_index]
    weights = picked / jnp.sum(picked)
    levels = level_table[threshold_index]

    def one_level(level):
        terms = weights[:, None, None] * (0.5 * (1.0 + jax.scipy.special.erf((level - height) * kernel_scale)))
        return jnp.sum(terms, axis=0)

    mixture_cdf = lax.map(one_level, levels)
    return height, mixture_cdf
```

```python
import jax
import jax.numpy as jnp
from jax import lax
from jax.sharding import PartitionSpec as P

ITERS = 8
NTHR = 16
NWEIGHT = 4

courant_half = 0.45
kernel_scale = 1.0 / (0.5 * 1.4142135623730951)

HALO = 2 * ITERS


def ring_pairs(count, shift, periodic):
    pairs = []
    for i in range(count):
        j = i + shift
        if periodic:
            j %= count
        elif not 0 <= j < count:
            continue
        pairs.append((i, j))
    return pairs


def grid_pairs(n_lon, n_lat, d_lon, d_lat):
    pairs = []
    for i in range(n_lon):
        for j in range(n_lat):
            tj = j + d_lat
            if not 0 <= tj < n_lat:
                continue
            ti = (i + d_lon) % n_lon
            pairs.append((i * n_lat + j, ti * n_lat + tj))
    return pairs


def with_halo(block):
    w = HALO
    n_lon = lax.axis_size("lon")
    n_lat = lax.axis_size("lat")
    both = ("lon", "lat")

    def send(piece, d_lon, d_lat):
        if d_lat == 0:
            return lax.ppermute(piece, "lon", ring_pairs(n_lon, d_lon, True))
        if d_lon == 0:
            return lax.ppermute(piece, "lat", ring_pairs(n_lat, d_lat, False))
        return lax.ppermute(piece, both, grid_pairs(n_lon, n_lat, d_lon, d_lat))

    lo_x = slice(-w, None)
    hi_x = slice(0, w)
    all_ = slice(None)
    parts = {}
    for dx, sx in ((-1, hi_x), (0, all_), (1, lo_x)):
        for dy, sy in ((-1, slice(0, w)), (0, all_), (1, slice(-w, None))):
            piece = block[..., sx, sy]
            if dx == 0 and dy == 0:
                parts[(0, 0)] = piece
            else:
                parts[(-dx, -dy)] = send(piece, dx, dy)
    rows = []
    for px in (-1, 0, 1):
        rows.append(jnp.concatenate([parts[(px, -1)], parts[(px, 0)], parts[(px, 1)]], axis=-1))
    return jnp.concatenate(rows, axis=-2)


def kernel_term(weight_one, levels, field):
    return weight_one * (
        0.5
        * (1.0 + jax.scipy.special.erf((levels[:, None, None] - field[None, :, :]) * kernel_scale))
    )


def shards(
    height, east, north, depth, coriolis, weight_table, member_index, level_table, threshold_index
):
    local_members, n_x, n_y = height.shape
    w = HALO
    stack = jnp.concatenate([height, east, north, depth[None], coriolis[None]], axis=0)
    wide = with_halo(stack)
    m = local_members
    h = wide[:m]
    e = wide[m : 2 * m]
    n = wide[2 * m : 3 * m]
    dep = wide[3 * m]
    cor = wide[3 * m + 1]

    n_lat_total = n_y * lax.axis_size("lat")
    lat0 = lax.axis_index("lat") * n_y - w

    off = 0
    for step in range(ITERS):
        d = dep[off : dep.shape[0] - off, off : dep.shape[1] - off]
        c = cor[off : cor.shape[0] - off, off : cor.shape[1] - off]
        fe = d * e
        fn = d * n
        hn = h[:, 1:-1, 1:-1] - courant_half * (
            (fe[:, 2:, 1:-1] - fe[:, :-2, 1:-1]) + (fn[:, 1:-1, 2:] - fn[:, 1:-1, :-2])
        )
        cols = lat0 + off + 1 + lax.broadcasted_iota(jnp.int32, (1, 1, hn.shape[2]), 2)
        inside = (cols >= 0) & (cols < n_lat_total)
        hn = jnp.where(inside, hn, 0.0)
        en = (
            e[:, 2:-2, 1:-1]
            + c[None, 2:-2, 1:-1] * n[:, 2:-2, 1:-1]
            - courant_half * (hn[:, 2:, :] - hn[:, :-2, :])
        )
        nn = (
            n[:, 2:-2, 2:-2]
            - c[None, 2:-2, 2:-2] * en[:, :, 1:-1]
            - courant_half * (hn[:, 1:-1, 2:] - hn[:, 1:-1, :-2])
        )
        h = hn[:, 1:-1, 1:-1]
        e = en[:, :, 1:-1]
        n = nn
        off += 2
    height = h

    picked = jnp.sum(
        jnp.where(
            member_index[:, None] == jnp.arange(NWEIGHT, dtype=jnp.int32)[None, :],
            weight_table[None, :],
            0.0,
        ),
        axis=1,
    )
    weights = picked / jnp.sum(picked)
    levels = jnp.sum(
        jnp.where(
            threshold_index[:, None] == jnp.arange(NTHR, dtype=jnp.int32)[None, :],
            level_table[None, :],
            0.0,
        ),
        axis=1,
    )
    n_mem = lax.axis_size("mem")
    assert n_mem == 2
    g = lax.axis_index("mem")
    own_rows = NTHR // n_mem
    own_weights = lax.dynamic_slice_in_dim(weights, g * local_members, local_members)
    own_levels = lax.dynamic_slice_in_dim(levels, g * own_rows, own_rows)
    other_levels = lax.dynamic_slice_in_dim(levels, (1 - g) * own_rows, own_rows)

    def partial(lv):
        total = kernel_term(own_weights[0], lv, height[0])
        for member in range(1, local_members):
            total = total + kernel_term(own_weights[member], lv, height[member])
        return total

    sent = lax.ppermute(partial(other_levels), "mem", [(0, 1), (1, 0)])
    mixture_cdf = partial(own_levels) + sent
    return (height, mixture_cdf)


def solution(mesh):
    in_specs = (
        P("mem", "lon", "lat"),
        P("mem", "lon", "lat"),
        P("mem", "lon", "lat"),
        P("lon", "lat"),
        P("lon", "lat"),
        P(),
        P(),
        P(),
        P(),
    )
    out_specs = (P("mem", "lon", "lat"), P("mem", "lon", "lat"))
    return jax.shard_map(shards, mesh=mesh, in_specs=in_specs, out_specs=out_specs, check_vma=False)
```

```python
import jax
import jax.numpy as jnp
from jax import lax
from jax.sharding import PartitionSpec as P

ITERS = 8
NTHR = 16
NWEIGHT = 4

courant_half = 0.45
kernel_scale = 1.0 / (0.5 * 1.4142135623730951)

HALO = 2 * ITERS


def ring_pairs(count, shift, periodic):
    pairs = []
    for i in range(count):
        j = i + shift
        if periodic:
            j %= count
        elif not 0 <= j < count:
            continue
        pairs.append((i, j))
    return pairs


def grid_pairs(n_lon, n_lat, d_lon, d_lat):
    pairs = []
    for i in range(n_lon):
        for j in range(n_lat):
            tj = j + d_lat
            if not 0 <= tj < n_lat:
                continue
            ti = (i + d_lon) % n_lon
            pairs.append((i * n_lat + j, ti * n_lat + tj))
    return pairs


def with_halo(fields):
    w = HALO
    n_lon = lax.axis_size("lon")
    n_lat = lax.axis_size("lat")
    both = ("lon", "lat")

    def send(piece, d_lon, d_lat):
        if d_lat == 0:
            return lax.ppermute(piece, "lon", ring_pairs(n_lon, d_lon, True))
        if d_lon == 0:
            return lax.ppermute(piece, "lat", ring_pairs(n_lat, d_lat, False))
        return lax.ppermute(piece, both, grid_pairs(n_lon, n_lat, d_lon, d_lat))

    flat = [f.reshape((-1,) + f.shape[-2:]) for f in fields]
    planes = [f.shape[0] for f in flat]
    all_ = slice(None)
    parts = {}
    for dx, sx in ((-1, slice(0, w)), (0, all_), (1, slice(-w, None))):
        for dy, sy in ((-1, slice(0, w)), (0, all_), (1, slice(-w, None))):
            if dx == 0 and dy == 0:
                continue
            piece = jnp.concatenate([f[:, sx, sy] for f in flat], axis=0)
            shape = piece.shape
            if dy != 0:
                piece = piece.reshape(-1, 128)
            got = send(piece, dx, dy)
            parts[(-dx, -dy)] = got.reshape(shape)
    out = []
    start = 0
    for f, count in zip(flat, planes):
        def cut(p):
            return p[start : start + count]
        rows = []
        for px in (-1, 0, 1):
            mid = f if px == 0 else cut(parts[(px, 0)])
            rows.append(jnp.concatenate([cut(parts[(px, -1)]), mid, cut(parts[(px, 1)])], axis=-1))
        start += count
        out.append(jnp.concatenate(rows, axis=-2))
    return [o.reshape(fi.shape[:-2] + o.shape[-2:]) for o, fi in zip(out, fields)]


def kernel_term(weight_one, levels, field):
    return weight_one * (
        0.5
        * (1.0 + jax.scipy.special.erf((levels[:, None, None] - field[None, :, :]) * kernel_scale))
    )


def shards(
    height, east, north, depth, coriolis, weight_table, member_index, level_table, threshold_index
):
    local_members, n_x, n_y = height.shape
    w = HALO
    h, e, n, dep, cor = with_halo([height, east, north, depth, coriolis])

    n_lat_total = n_y * lax.axis_size("lat")
    lat0 = lax.axis_index("lat") * n_y - w

    off = 0
    for step in range(ITERS):
        d = dep[off : dep.shape[0] - off, off : dep.shape[1] - off]
        c = cor[off : cor.shape[0] - off, off : cor.shape[1] - off]
        fe = d * e
        fn = d * n
        hn = h[:, 1:-1, 1:-1] - courant_half * (
            (fe[:, 2:, 1:-1] - fe[:, :-2, 1:-1]) + (fn[:, 1:-1, 2:] - fn[:, 1:-1, :-2])
        )
        cols = lat0 + off + 1 + lax.broadcasted_iota(jnp.int32, (1, 1, hn.shape[2]), 2)
        inside = (cols >= 0) & (cols < n_lat_total)
        hn = jnp.where(inside, hn, 0.0)
        en = (
            e[:, 2:-2, 1:-1]
            + c[None, 2:-2, 1:-1] * n[:, 2:-2, 1:-1]
            - courant_half * (hn[:, 2:, :] - hn[:, :-2, :])
        )
        nn = (
            n[:, 2:-2, 2:-2]
            - c[None, 2:-2, 2:-2] * en[:, :, 1:-1]
            - courant_half * (hn[:, 1:-1, 2:] - hn[:, 1:-1, :-2])
        )
        h = hn[:, 1:-1, 1:-1]
        e = en[:, :, 1:-1]
        n = nn
        off += 2
    height = h

    picked = jnp.sum(
        jnp.where(
            member_index[:, None] == jnp.arange(NWEIGHT, dtype=jnp.int32)[None, :],
            weight_table[None, :],
            0.0,
        ),
        axis=1,
    )
    weights = picked / jnp.sum(picked)
    levels = jnp.sum(
        jnp.where(
            threshold_index[:, None] == jnp.arange(NTHR, dtype=jnp.int32)[None, :],
            level_table[None, :],
            0.0,
        ),
        axis=1,
    )
    n_mem = lax.axis_size("mem")
    assert n_mem == 2
    g = lax.axis_index("mem")
    own_rows = NTHR // n_mem
    own_weights = lax.dynamic_slice_in_dim(weights, g * local_members, local_members)
    own_levels = lax.dynamic_slice_in_dim(levels, g * own_rows, own_rows)
    other_levels = lax.dynamic_slice_in_dim(levels, (1 - g) * own_rows, own_rows)

    def partial(lv):
        total = kernel_term(own_weights[0], lv, height[0])
        for member in range(1, local_members):
            total = total + kernel_term(own_weights[member], lv, height[member])
        return total

    sent = lax.ppermute(partial(other_levels), "mem", [(0, 1), (1, 0)])
    mixture_cdf = partial(own_levels) + sent
    return (height, mixture_cdf)


def solution(mesh):
    in_specs = (
        P("mem", "lon", "lat"),
        P("mem", "lon", "lat"),
        P("mem", "lon", "lat"),
        P("lon", "lat"),
        P("lon", "lat"),
        P(),
        P(),
        P(),
        P(),
    )
    out_specs = (P("mem", "lon", "lat"), P("mem", "lon", "lat"))
    return jax.shard_map(shards, mesh=mesh, in_specs=in_specs, out_specs=out_specs, check_vma=False)
```

```python
import jax
import jax.numpy as jnp
from jax import lax
from jax.sharding import PartitionSpec as P

ITERS = 8
NTHR = 16
NWEIGHT = 4

courant_half = 0.45
kernel_scale = 1.0 / (0.5 * 1.4142135623730951)

HALO = 2 * ITERS


def ring_pairs(count, shift, periodic):
    pairs = []
    for i in range(count):
        j = i + shift
        if periodic:
            j %= count
        elif not 0 <= j < count:
            continue
        pairs.append((i, j))
    return pairs


def grid_pairs(n_lon, n_lat, d_lon, d_lat):
    pairs = []
    for i in range(n_lon):
        for j in range(n_lat):
            tj = j + d_lat
            if not 0 <= tj < n_lat:
                continue
            ti = (i + d_lon) % n_lon
            pairs.append((i * n_lat + j, ti * n_lat + tj))
    return pairs


def with_halo(fields):
    w = HALO
    n_lon = lax.axis_size("lon")
    n_lat = lax.axis_size("lat")
    flat = [f.reshape((-1,) + f.shape[-2:]) for f in fields]
    planes = [f.shape[0] for f in flat]
    block = jnp.concatenate(flat, axis=0)
    low = lax.ppermute(block[:, -w:, :], "lon", ring_pairs(n_lon, 1, True))
    high = lax.ppermute(block[:, :w, :], "lon", ring_pairs(n_lon, -1, True))
    block = jnp.concatenate([low, block, high], axis=1)

    def lat_send(piece, shift):
        got = lax.ppermute(piece.reshape(-1, 128), "lat", ring_pairs(n_lat, shift, False))
        return got.reshape(piece.shape)

    low = lat_send(block[:, :, -w:], 1)
    high = lat_send(block[:, :, :w], -1)
    block = jnp.concatenate([low, block, high], axis=2)
    out = []
    start = 0
    for f, count in zip(fields, planes):
        out.append(block[start : start + count].reshape(f.shape[:-2] + block.shape[-2:]))
        start += count
    return out


def kernel_term(weight_one, levels, field):
    return weight_one * (
        0.5
        * (1.0 + jax.scipy.special.erf((levels[:, None, None] - field[None, :, :]) * kernel_scale))
    )


def shards(
    height, east, north, depth, coriolis, weight_table, member_index, level_table, threshold_index
):
    local_members, n_x, n_y = height.shape
    w = HALO
    h, e, n, dep, cor = with_halo([height, east, north, depth, coriolis])

    n_lat_total = n_y * lax.axis_size("lat")
    lat0 = lax.axis_index("lat") * n_y - w

    off = 0
    for step in range(ITERS):
        d = dep[off : dep.shape[0] - off, off : dep.shape[1] - off]
        c = cor[off : cor.shape[0] - off, off : cor.shape[1] - off]
        fe = d * e
        fn = d * n
        hn = h[:, 1:-1, 1:-1] - courant_half * (
            (fe[:, 2:, 1:-1] - fe[:, :-2, 1:-1]) + (fn[:, 1:-1, 2:] - fn[:, 1:-1, :-2])
        )
        cols = lat0 + off + 1 + lax.broadcasted_iota(jnp.int32, (1, 1, hn.shape[2]), 2)
        inside = (cols >= 0) & (cols < n_lat_total)
        hn = jnp.where(inside, hn, 0.0)
        en = (
            e[:, 2:-2, 1:-1]
            + c[None, 2:-2, 1:-1] * n[:, 2:-2, 1:-1]
            - courant_half * (hn[:, 2:, :] - hn[:, :-2, :])
        )
        nn = (
            n[:, 2:-2, 2:-2]
            - c[None, 2:-2, 2:-2] * en[:, :, 1:-1]
            - courant_half * (hn[:, 1:-1, 2:] - hn[:, 1:-1, :-2])
        )
        h = hn[:, 1:-1, 1:-1]
        e = en[:, :, 1:-1]
        n = nn
        off += 2
    height = h

    picked = jnp.sum(
        jnp.where(
            member_index[:, None] == jnp.arange(NWEIGHT, dtype=jnp.int32)[None, :],
            weight_table[None, :],
            0.0,
        ),
        axis=1,
    )
    weights = picked / jnp.sum(picked)
    levels = jnp.sum(
        jnp.where(
            threshold_index[:, None] == jnp.arange(NTHR, dtype=jnp.int32)[None, :],
            level_table[None, :],
            0.0,
        ),
        axis=1,
    )
    n_mem = lax.axis_size("mem")
    assert n_mem == 2
    g = lax.axis_index("mem")
    own_rows = NTHR // n_mem
    own_weights = lax.dynamic_slice_in_dim(weights, g * local_members, local_members)
    own_levels = lax.dynamic_slice_in_dim(levels, g * own_rows, own_rows)
    other_levels = lax.dynamic_slice_in_dim(levels, (1 - g) * own_rows, own_rows)

    def partial(lv):
        total = kernel_term(own_weights[0], lv, height[0])
        for member in range(1, local_members):
            total = total + kernel_term(own_weights[member], lv, height[member])
        return total

    sent = lax.ppermute(partial(other_levels), "mem", [(0, 1), (1, 0)])
    mixture_cdf = partial(own_levels) + sent
    return (height, mixture_cdf)


def solution(mesh):
    in_specs = (
        P("mem", "lon", "lat"),
        P("mem", "lon", "lat"),
        P("mem", "lon", "lat"),
        P("lon", "lat"),
        P("lon", "lat"),
        P(),
        P(),
        P(),
        P(),
    )
    out_specs = (P("mem", "lon", "lat"), P("mem", "lon", "lat"))
    return jax.shard_map(shards, mesh=mesh, in_specs=in_specs, out_specs=out_specs, check_vma=False)
```

```python
import jax
import jax.numpy as jnp
from jax import lax
from jax.sharding import PartitionSpec as P
from jax.experimental import pallas as pl
from jax.experimental.pallas import tpu as pltpu

ITERS = 8
NTHR = 16
NWEIGHT = 4

courant_half = 0.45
kernel_scale = 1.0 / (0.5 * 1.4142135623730951)

HALO = 2 * ITERS


def ring_pairs(count, shift, periodic):
    pairs = []
    for i in range(count):
        j = i + shift
        if periodic:
            j %= count
        elif not 0 <= j < count:
            continue
        pairs.append((i, j))
    return pairs


def grid_pairs(n_lon, n_lat, d_lon, d_lat):
    pairs = []
    for i in range(n_lon):
        for j in range(n_lat):
            tj = j + d_lat
            if not 0 <= tj < n_lat:
                continue
            ti = (i + d_lon) % n_lon
            pairs.append((i * n_lat + j, ti * n_lat + tj))
    return pairs


LANES = 128


def with_halo(fields, pad_to):
    w = HALO
    n_lon = lax.axis_size("lon")
    n_lat = lax.axis_size("lat")
    flat = [f.reshape((-1,) + f.shape[-2:]) for f in fields]
    planes = [f.shape[0] for f in flat]
    block = jnp.concatenate(flat, axis=0)
    low = lax.ppermute(block[:, -w:, :], "lon", ring_pairs(n_lon, 1, True))
    high = lax.ppermute(block[:, :w, :], "lon", ring_pairs(n_lon, -1, True))
    block = jnp.concatenate([block, high, low], axis=1)

    def lat_send(piece, shift):
        got = lax.ppermute(piece.reshape(-1, LANES), "lat", ring_pairs(n_lat, shift, False))
        return got.reshape(piece.shape)

    low = lat_send(block[:, :, -w:], 1)
    high = lat_send(block[:, :, :w], -1)
    gap = jnp.zeros(block.shape[:2] + (pad_to - block.shape[2] - 2 * w,), block.dtype)
    return jnp.concatenate([block, high, gap, low], axis=2), planes


def steps_kernel(h_ref, e_ref, n_ref, d_ref, c_ref, inside_ref, out_ref):
    h = h_ref[...]
    e = e_ref[...]
    n = n_ref[...]
    d = d_ref[...]
    c = c_ref[...]
    inside = inside_ref[...] > 0.5
    rows, cols = h.shape

    def dx(q):
        return pltpu.roll(q, rows - 1, 0) - pltpu.roll(q, 1, 0)

    def dy(q):
        return pltpu.roll(q, cols - 1, 1) - pltpu.roll(q, 1, 1)

    for step in range(ITERS):
        fe = d * e
        fn = d * n
        h = h - courant_half * (dx(fe) + dy(fn))
        h = jnp.where(inside, h, 0.0)
        e = e + c * n - courant_half * dx(h)
        n = n - c * e - courant_half * dy(h)
    out_ref[...] = h[: out_ref.shape[0], : out_ref.shape[1]]


def run_steps(wide, planes, members, n_x, n_y, inside):
    _, rows, cols = wide.shape

    def member_spec(first):
        return pl.BlockSpec((None, rows, cols), lambda m: (first + m, 0, 0))

    def plane_spec(index):
        return pl.BlockSpec((None, rows, cols), lambda m: (index, 0, 0))

    per_elem = rows * cols * ITERS
    return pl.pallas_call(
        steps_kernel,
        grid=(members,),
        in_specs=[
            member_spec(0),
            member_spec(members),
            member_spec(2 * members),
            plane_spec(3 * members),
            plane_spec(3 * members + 1),
            pl.BlockSpec((1, cols), lambda m: (0, 0)),
        ],
        out_specs=pl.BlockSpec((None, n_x, n_y), lambda m: (m, 0, 0)),
        out_shape=jax.ShapeDtypeStruct((members, n_x, n_y), jnp.float32),
        cost_estimate=pl.CostEstimate(
            flops=20 * per_elem * members,
            transcendentals=0,
            bytes_accessed=4 * rows * cols * (3 * members + 2) + 4 * members * n_x * n_y,
        ),
    )(wide, wide, wide, wide, wide, inside)


def kernel_term(weight_one, levels, field):
    return weight_one * (
        0.5
        * (1.0 + jax.scipy.special.erf((levels[:, None, None] - field[None, :, :]) * kernel_scale))
    )


def shards(
    height, east, north, depth, coriolis, weight_table, member_index, level_table, threshold_index
):
    local_members, n_x, n_y = height.shape
    w = HALO
    m = local_members
    pad_to = -(-(n_y + 2 * w) // LANES) * LANES
    wide, planes = with_halo([height, east, north, depth, coriolis], pad_to)
    n_lat_total = n_y * lax.axis_size("lat")
    lane = jnp.arange(pad_to, dtype=jnp.int32)
    local = jnp.where(lane < n_y + w, lane, jnp.where(lane >= pad_to - w, lane - pad_to, -n_lat_total))
    cols = lax.axis_index("lat") * n_y + local
    real = (lane < n_y + w) | (lane >= pad_to - w)
    inside = (real & (cols >= 0) & (cols < n_lat_total)).astype(jnp.float32)[None, :]
    height = run_steps(wide, planes, m, n_x, n_y, inside)

    picked = jnp.sum(
        jnp.where(
            member_index[:, None] == jnp.arange(NWEIGHT, dtype=jnp.int32)[None, :],
            weight_table[None, :],
            0.0,
        ),
        axis=1,
    )
    weights = picked / jnp.sum(picked)
    levels = jnp.sum(
        jnp.where(
            threshold_index[:, None] == jnp.arange(NTHR, dtype=jnp.int32)[None, :],
            level_table[None, :],
            0.0,
        ),
        axis=1,
    )
    n_mem = lax.axis_size("mem")
    assert n_mem == 2
    g = lax.axis_index("mem")
    own_rows = NTHR // n_mem
    own_weights = lax.dynamic_slice_in_dim(weights, g * local_members, local_members)
    own_levels = lax.dynamic_slice_in_dim(levels, g * own_rows, own_rows)
    other_levels = lax.dynamic_slice_in_dim(levels, (1 - g) * own_rows, own_rows)

    def partial(lv):
        total = kernel_term(own_weights[0], lv, height[0])
        for member in range(1, local_members):
            total = total + kernel_term(own_weights[member], lv, height[member])
        return total

    sent = lax.ppermute(partial(other_levels), "mem", [(0, 1), (1, 0)])
    mixture_cdf = partial(own_levels) + sent
    return (height, mixture_cdf)


def solution(mesh):
    in_specs = (
        P("mem", "lon", "lat"),
        P("mem", "lon", "lat"),
        P("mem", "lon", "lat"),
        P("lon", "lat"),
        P("lon", "lat"),
        P(),
        P(),
        P(),
        P(),
    )
    out_specs = (P("mem", "lon", "lat"), P("mem", "lon", "lat"))
    return jax.shard_map(shards, mesh=mesh, in_specs=in_specs, out_specs=out_specs, check_vma=False)
```

```python
import jax
import jax.numpy as jnp
from jax import lax
from jax.sharding import PartitionSpec as P
from jax.experimental import pallas as pl
from jax.experimental.pallas import tpu as pltpu

ITERS = 8
NTHR = 16
NWEIGHT = 4

courant_half = 0.45
kernel_scale = 1.0 / (0.5 * 1.4142135623730951)

HALO = 2 * ITERS


def ring_pairs(count, shift, periodic):
    pairs = []
    for i in range(count):
        j = i + shift
        if periodic:
            j %= count
        elif not 0 <= j < count:
            continue
        pairs.append((i, j))
    return pairs


def grid_pairs(n_lon, n_lat, d_lon, d_lat):
    pairs = []
    for i in range(n_lon):
        for j in range(n_lat):
            tj = j + d_lat
            if not 0 <= tj < n_lat:
                continue
            ti = (i + d_lon) % n_lon
            pairs.append((i * n_lat + j, ti * n_lat + tj))
    return pairs


LANES = 128


def with_halo(fields, pad_to, after=None):
    w = HALO
    n_lon = lax.axis_size("lon")
    n_lat = lax.axis_size("lat")
    flat = [f.reshape((-1,) + f.shape[-2:]) for f in fields]
    planes = [f.shape[0] for f in flat]
    block = jnp.concatenate(flat, axis=0)
    if after is not None:
        block, _ = lax.optimization_barrier((block, after))
    low = lax.ppermute(block[:, -w:, :], "lon", ring_pairs(n_lon, 1, True))
    high = lax.ppermute(block[:, :w, :], "lon", ring_pairs(n_lon, -1, True))
    block = jnp.concatenate([block, high, low], axis=1)

    def lat_send(piece, shift):
        got = lax.ppermute(piece.reshape(-1, LANES), "lat", ring_pairs(n_lat, shift, False))
        return got.reshape(piece.shape)

    low = lat_send(block[:, :, -w:], 1)
    high = lat_send(block[:, :, :w], -1)
    gap = jnp.zeros(block.shape[:2] + (pad_to - block.shape[2] - 2 * w,), block.dtype)
    return jnp.concatenate([block, high, gap, low], axis=2), planes


def steps_kernel(h_ref, e_ref, n_ref, d_ref, c_ref, inside_ref, out_ref):
    h = h_ref[...]
    e = e_ref[...]
    n = n_ref[...]
    d = d_ref[...]
    c = c_ref[...]
    inside = inside_ref[...] > 0.5
    rows, cols = h.shape

    def dx(q):
        return pltpu.roll(q, rows - 1, 0) - pltpu.roll(q, 1, 0)

    def dy(q):
        return pltpu.roll(q, cols - 1, 1) - pltpu.roll(q, 1, 1)

    for step in range(ITERS):
        fe = d * e
        fn = d * n
        h = h - courant_half * (dx(fe) + dy(fn))
        h = jnp.where(inside, h, 0.0)
        e = e + c * n - courant_half * dx(h)
        n = n - c * e - courant_half * dy(h)
    out_ref[...] = h[: out_ref.shape[0], : out_ref.shape[1]]


def run_steps(wide, statics, first_static, members, n_x, n_y, inside):
    _, rows, cols = wide.shape

    def member_spec(first):
        return pl.BlockSpec((None, rows, cols), lambda m: (first + m, 0, 0))

    def plane_spec(index):
        return pl.BlockSpec((None, rows, cols), lambda m: (index, 0, 0))

    per_elem = rows * cols * ITERS
    return pl.pallas_call(
        steps_kernel,
        grid=(members,),
        in_specs=[
            member_spec(0),
            member_spec(members),
            member_spec(2 * members),
            plane_spec(first_static),
            plane_spec(first_static + 1),
            pl.BlockSpec((1, cols), lambda m: (0, 0)),
        ],
        out_specs=pl.BlockSpec((None, n_x, n_y), lambda m: (m, 0, 0)),
        out_shape=jax.ShapeDtypeStruct((members, n_x, n_y), jnp.float32),
        cost_estimate=pl.CostEstimate(
            flops=20 * per_elem * members,
            transcendentals=0,
            bytes_accessed=4 * rows * cols * (3 * members + 1) + 4 * members * n_x * n_y,
        ),
    )(wide, wide, wide, statics, statics, inside)


def kernel_term(weight_one, levels, field):
    return weight_one * (
        0.5
        * (1.0 + jax.scipy.special.erf((levels[:, None, None] - field[None, :, :]) * kernel_scale))
    )


def shards(
    height, east, north, depth, coriolis, weight_table, member_index, level_table, threshold_index
):
    local_members, n_x, n_y = height.shape
    w = HALO
    m = local_members
    pad_to = -(-(n_y + 2 * w) // LANES) * LANES
    cm = m // 2
    wide_a, _ = with_halo([height[:cm], east[:cm], north[:cm], depth, coriolis], pad_to)
    wide_b, _ = with_halo([height[cm:], east[cm:], north[cm:]], pad_to, after=wide_a)
    n_lat_total = n_y * lax.axis_size("lat")
    lane = jnp.arange(pad_to, dtype=jnp.int32)
    local = jnp.where(lane < n_y + w, lane, jnp.where(lane >= pad_to - w, lane - pad_to, -n_lat_total))
    cols = lax.axis_index("lat") * n_y + local
    real = (lane < n_y + w) | (lane >= pad_to - w)
    inside = (real & (cols >= 0) & (cols < n_lat_total)).astype(jnp.float32)[None, :]
    height_a = run_steps(wide_a, wide_a, 3 * cm, cm, n_x, n_y, inside)
    height_b = run_steps(wide_b, wide_a, 3 * cm, m - cm, n_x, n_y, inside)
    height = jnp.concatenate([height_a, height_b], axis=0)

    picked = jnp.sum(
        jnp.where(
            member_index[:, None] == jnp.arange(NWEIGHT, dtype=jnp.int32)[None, :],
            weight_table[None, :],
            0.0,
        ),
        axis=1,
    )
    weights = picked / jnp.sum(picked)
    levels = jnp.sum(
        jnp.where(
            threshold_index[:, None] == jnp.arange(NTHR, dtype=jnp.int32)[None, :],
            level_table[None, :],
            0.0,
        ),
        axis=1,
    )
    n_mem = lax.axis_size("mem")
    assert n_mem == 2
    g = lax.axis_index("mem")
    own_rows = NTHR // n_mem
    own_weights = lax.dynamic_slice_in_dim(weights, g * local_members, local_members)
    own_levels = lax.dynamic_slice_in_dim(levels, g * own_rows, own_rows)
    other_levels = lax.dynamic_slice_in_dim(levels, (1 - g) * own_rows, own_rows)

    def partial(lv, field, first):
        total = kernel_term(own_weights[first], lv, field[0])
        for member in range(1, field.shape[0]):
            total = total + kernel_term(own_weights[first + member], lv, field[member])
        return total

    swap = [(0, 1), (1, 0)]
    sent_a = lax.ppermute(partial(other_levels, height_a, 0), "mem", swap)
    sent_b = lax.ppermute(partial(other_levels, height_b, cm), "mem", swap)
    mixture_cdf = (partial(own_levels, height_a, 0) + partial(own_levels, height_b, cm)) + (
        sent_a + sent_b
    )
    return (height, mixture_cdf)


def solution(mesh):
    in_specs = (
        P("mem", "lon", "lat"),
        P("mem", "lon", "lat"),
        P("mem", "lon", "lat"),
        P("lon", "lat"),
        P("lon", "lat"),
        P(),
        P(),
        P(),
        P(),
    )
    out_specs = (P("mem", "lon", "lat"), P("mem", "lon", "lat"))
    return jax.shard_map(shards, mesh=mesh, in_specs=in_specs, out_specs=out_specs, check_vma=False)
```

```python
import jax
import jax.numpy as jnp
from jax import lax
from jax.sharding import PartitionSpec as P
from jax.experimental import pallas as pl
from jax.experimental.pallas import tpu as pltpu

ITERS = 8
NTHR = 16
NWEIGHT = 4

courant_half = 0.45
kernel_scale = 1.0 / (0.5 * 1.4142135623730951)

HALO = 2 * ITERS


def ring_pairs(count, shift, periodic):
    pairs = []
    for i in range(count):
        j = i + shift
        if periodic:
            j %= count
        elif not 0 <= j < count:
            continue
        pairs.append((i, j))
    return pairs


def grid_pairs(n_lon, n_lat, d_lon, d_lat):
    pairs = []
    for i in range(n_lon):
        for j in range(n_lat):
            tj = j + d_lat
            if not 0 <= tj < n_lat:
                continue
            ti = (i + d_lon) % n_lon
            pairs.append((i * n_lat + j, ti * n_lat + tj))
    return pairs


LANES = 128


def with_halo(fields, pad_to):
    w = HALO
    n_lon = lax.axis_size("lon")
    n_lat = lax.axis_size("lat")
    flat = [f.reshape((-1,) + f.shape[-2:]) for f in fields]
    planes = [f.shape[0] for f in flat]

    def stack(sx, sy):
        return jnp.concatenate([f[:, sx, sy] for f in flat], axis=0)

    everything = slice(None)
    low_x = lax.ppermute(stack(slice(-w, None), everything), "lon", ring_pairs(n_lon, 1, True))
    high_x = lax.ppermute(stack(slice(0, w), everything), "lon", ring_pairs(n_lon, -1, True))

    def lat_send(sy, shift):
        piece = jnp.concatenate([stack(everything, sy), high_x[:, :, sy], low_x[:, :, sy]], axis=1)
        got = lax.ppermute(piece.reshape(-1, LANES), "lat", ring_pairs(n_lat, shift, False))
        return got.reshape(piece.shape)

    low_y = lat_send(slice(-w, None), 1)
    high_y = lat_send(slice(0, w), -1)
    block = jnp.concatenate([stack(everything, everything), high_x, low_x], axis=1)
    gap = jnp.zeros(block.shape[:2] + (pad_to - block.shape[2] - 2 * w,), block.dtype)
    return jnp.concatenate([block, high_y, gap, low_y], axis=2), planes


def steps_kernel(h_ref, e_ref, n_ref, d_ref, c_ref, inside_ref, out_ref):
    h = h_ref[...]
    e = e_ref[...]
    n = n_ref[...]
    d = d_ref[...]
    c = c_ref[...]
    inside = inside_ref[...] > 0.5
    rows, cols = h.shape

    def dx(q):
        return pltpu.roll(q, rows - 1, 0) - pltpu.roll(q, 1, 0)

    def dy(q):
        return pltpu.roll(q, cols - 1, 1) - pltpu.roll(q, 1, 1)

    for step in range(ITERS):
        fe = d * e
        fn = d * n
        h = h - courant_half * (dx(fe) + dy(fn))
        h = jnp.where(inside, h, 0.0)
        e = e + c * n - courant_half * dx(h)
        n = n - c * e - courant_half * dy(h)
    out_ref[...] = h[: out_ref.shape[0], : out_ref.shape[1]]


def run_steps(wide, planes, members, n_x, n_y, inside):
    _, rows, cols = wide.shape

    def member_spec(first):
        return pl.BlockSpec((None, rows, cols), lambda m: (first + m, 0, 0))

    def plane_spec(index):
        return pl.BlockSpec((None, rows, cols), lambda m: (index, 0, 0))

    per_elem = rows * cols * ITERS
    return pl.pallas_call(
        steps_kernel,
        grid=(members,),
        in_specs=[
            member_spec(0),
            member_spec(members),
            member_spec(2 * members),
            plane_spec(3 * members),
            plane_spec(3 * members + 1),
            pl.BlockSpec((1, cols), lambda m: (0, 0)),
        ],
        out_specs=pl.BlockSpec((None, n_x, n_y), lambda m: (m, 0, 0)),
        out_shape=jax.ShapeDtypeStruct((members, n_x, n_y), jnp.float32),
        cost_estimate=pl.CostEstimate(
            flops=20 * per_elem * members,
            transcendentals=0,
            bytes_accessed=4 * rows * cols * (3 * members + 2) + 4 * members * n_x * n_y,
        ),
    )(wide, wide, wide, wide, wide, inside)


def kernel_term(weight_one, levels, field):
    return weight_one * (
        0.5
        * (1.0 + jax.scipy.special.erf((levels[:, None, None] - field[None, :, :]) * kernel_scale))
    )


def shards(
    height, east, north, depth, coriolis, weight_table, member_index, level_table, threshold_index
):
    local_members, n_x, n_y = height.shape
    w = HALO
    m = local_members
    pad_to = -(-(n_y + 2 * w) // LANES) * LANES
    wide, planes = with_halo([height, east, north, depth, coriolis], pad_to)
    n_lat_total = n_y * lax.axis_size("lat")
    lane = jnp.arange(pad_to, dtype=jnp.int32)
    local = jnp.where(lane < n_y + w, lane, jnp.where(lane >= pad_to - w, lane - pad_to, -n_lat_total))
    cols = lax.axis_index("lat") * n_y + local
    real = (lane < n_y + w) | (lane >= pad_to - w)
    inside = (real & (cols >= 0) & (cols < n_lat_total)).astype(jnp.float32)[None, :]
    height = run_steps(wide, planes, m, n_x, n_y, inside)

    picked = jnp.sum(
        jnp.where(
            member_index[:, None] == jnp.arange(NWEIGHT, dtype=jnp.int32)[None, :],
            weight_table[None, :],
            0.0,
        ),
        axis=1,
    )
    weights = picked / jnp.sum(picked)
    levels = jnp.sum(
        jnp.where(
            threshold_index[:, None] == jnp.arange(NTHR, dtype=jnp.int32)[None, :],
            level_table[None, :],
            0.0,
        ),
        axis=1,
    )
    n_mem = lax.axis_size("mem")
    assert n_mem == 2
    g = lax.axis_index("mem")
    own_rows = NTHR // n_mem
    own_weights = lax.dynamic_slice_in_dim(weights, g * local_members, local_members)
    own_levels = lax.dynamic_slice_in_dim(levels, g * own_rows, own_rows)
    other_levels = lax.dynamic_slice_in_dim(levels, (1 - g) * own_rows, own_rows)

    def partial(lv):
        total = kernel_term(own_weights[0], lv, height[0])
        for member in range(1, local_members):
            total = total + kernel_term(own_weights[member], lv, height[member])
        return total

    sent = lax.ppermute(partial(other_levels), "mem", [(0, 1), (1, 0)])
    mixture_cdf = partial(own_levels) + sent
    return (height, mixture_cdf)


def solution(mesh):
    in_specs = (
        P("mem", "lon", "lat"),
        P("mem", "lon", "lat"),
        P("mem", "lon", "lat"),
        P("lon", "lat"),
        P("lon", "lat"),
        P(),
        P(),
        P(),
        P(),
    )
    out_specs = (P("mem", "lon", "lat"), P("mem", "lon", "lat"))
    return jax.shard_map(shards, mesh=mesh, in_specs=in_specs, out_specs=out_specs, check_vma=False)
```

```python
import jax
import jax.numpy as jnp
from jax import lax
from jax.sharding import PartitionSpec as P

ITERS = 8
NTHR = 16
NWEIGHT = 4

courant_half = 0.45
kernel_scale = 1.0 / (0.5 * 1.4142135623730951)

HALO = 2 * ITERS


def ring_pairs(count, shift, periodic):
    pairs = []
    for i in range(count):
        j = i + shift
        if periodic:
            j %= count
        elif not 0 <= j < count:
            continue
        pairs.append((i, j))
    return pairs


def grid_pairs(n_lon, n_lat, d_lon, d_lat):
    pairs = []
    for i in range(n_lon):
        for j in range(n_lat):
            tj = j + d_lat
            if not 0 <= tj < n_lat:
                continue
            ti = (i + d_lon) % n_lon
            pairs.append((i * n_lat + j, ti * n_lat + tj))
    return pairs


def with_halo(fields):
    w = HALO
    n_lon = lax.axis_size("lon")
    n_lat = lax.axis_size("lat")
    flat = [f.reshape((-1,) + f.shape[-2:]) for f in fields]
    planes = [f.shape[0] for f in flat]
    block = jnp.concatenate(flat, axis=0)
    low = lax.ppermute(block[:, -w:, :], "lon", ring_pairs(n_lon, 1, True))
    high = lax.ppermute(block[:, :w, :], "lon", ring_pairs(n_lon, -1, True))
    block = jnp.concatenate([low, block, high], axis=1)

    def lat_swap(piece, pairs):
        got = lax.ppermute(piece.reshape(-1, 128), "lat", pairs)
        return got.reshape(piece.shape)

    even = lax.rem(lax.axis_index("lat"), 2) == 0
    first_side = jnp.where(even, block[:, :, -w:], block[:, :, :w])
    second_side = jnp.where(even, block[:, :, :w], block[:, :, -w:])
    inner = [(i, i ^ 1) for i in range(n_lat - n_lat % 2)]
    outer = [(i, i + 1 if i % 2 else i - 1) for i in range(1, n_lat - 1)]
    got_first = lat_swap(first_side, inner)
    got_second = lat_swap(second_side, outer)
    low = jnp.where(even, got_second, got_first)
    high = jnp.where(even, got_first, got_second)
    block = jnp.concatenate([low, block, high], axis=2)
    out = []
    start = 0
    for f, count in zip(fields, planes):
        out.append(block[start : start + count].reshape(f.shape[:-2] + block.shape[-2:]))
        start += count
    return out


def kernel_term(weight_one, levels, field):
    return weight_one * (
        0.5
        * (1.0 + jax.scipy.special.erf((levels[:, None, None] - field[None, :, :]) * kernel_scale))
    )


def shards(
    height, east, north, depth, coriolis, weight_table, member_index, level_table, threshold_index
):
    local_members, n_x, n_y = height.shape
    w = HALO
    h, e, n, dep, cor = with_halo([height, east, north, depth, coriolis])

    n_lat_total = n_y * lax.axis_size("lat")
    lat0 = lax.axis_index("lat") * n_y - w

    off = 0
    for step in range(ITERS):
        d = dep[off : dep.shape[0] - off, off : dep.shape[1] - off]
        c = cor[off : cor.shape[0] - off, off : cor.shape[1] - off]
        fe = d * e
        fn = d * n
        hn = h[:, 1:-1, 1:-1] - courant_half * (
            (fe[:, 2:, 1:-1] - fe[:, :-2, 1:-1]) + (fn[:, 1:-1, 2:] - fn[:, 1:-1, :-2])
        )
        cols = lat0 + off + 1 + lax.broadcasted_iota(jnp.int32, (1, 1, hn.shape[2]), 2)
        inside = (cols >= 0) & (cols < n_lat_total)
        hn = jnp.where(inside, hn, 0.0)
        en = (
            e[:, 2:-2, 1:-1]
            + c[None, 2:-2, 1:-1] * n[:, 2:-2, 1:-1]
            - courant_half * (hn[:, 2:, :] - hn[:, :-2, :])
        )
        nn = (
            n[:, 2:-2, 2:-2]
            - c[None, 2:-2, 2:-2] * en[:, :, 1:-1]
            - courant_half * (hn[:, 1:-1, 2:] - hn[:, 1:-1, :-2])
        )
        h = hn[:, 1:-1, 1:-1]
        e = en[:, :, 1:-1]
        n = nn
        off += 2
    height = h

    picked = jnp.sum(
        jnp.where(
            member_index[:, None] == jnp.arange(NWEIGHT, dtype=jnp.int32)[None, :],
            weight_table[None, :],
            0.0,
        ),
        axis=1,
    )
    weights = picked / jnp.sum(picked)
    levels = jnp.sum(
        jnp.where(
            threshold_index[:, None] == jnp.arange(NTHR, dtype=jnp.int32)[None, :],
            level_table[None, :],
            0.0,
        ),
        axis=1,
    )
    n_mem = lax.axis_size("mem")
    assert n_mem == 2
    g = lax.axis_index("mem")
    own_rows = NTHR // n_mem
    own_weights = lax.dynamic_slice_in_dim(weights, g * local_members, local_members)
    own_levels = lax.dynamic_slice_in_dim(levels, g * own_rows, own_rows)
    other_levels = lax.dynamic_slice_in_dim(levels, (1 - g) * own_rows, own_rows)

    def partial(lv):
        total = kernel_term(own_weights[0], lv, height[0])
        for member in range(1, local_members):
            total = total + kernel_term(own_weights[member], lv, height[member])
        return total

    sent = lax.ppermute(partial(other_levels), "mem", [(0, 1), (1, 0)])
    mixture_cdf = partial(own_levels) + sent
    return (height, mixture_cdf)


def solution(mesh):
    in_specs = (
        P("mem", "lon", "lat"),
        P("mem", "lon", "lat"),
        P("mem", "lon", "lat"),
        P("lon", "lat"),
        P("lon", "lat"),
        P(),
        P(),
        P(),
        P(),
    )
    out_specs = (P("mem", "lon", "lat"), P("mem", "lon", "lat"))
    return jax.shard_map(shards, mesh=mesh, in_specs=in_specs, out_specs=out_specs, check_vma=False)
```

```python
import jax
import jax.numpy as jnp
from jax import lax
from jax.sharding import PartitionSpec as P

ITERS = 8
NTHR = 16
NWEIGHT = 4

courant_half = 0.45
kernel_scale = 1.0 / (0.5 * 1.4142135623730951)

HALO = 2 * ITERS


def ring_pairs(count, shift, periodic):
    pairs = []
    for i in range(count):
        j = i + shift
        if periodic:
            j %= count
        elif not 0 <= j < count:
            continue
        pairs.append((i, j))
    return pairs


def grid_pairs(n_lon, n_lat, d_lon, d_lat):
    pairs = []
    for i in range(n_lon):
        for j in range(n_lat):
            tj = j + d_lat
            if not 0 <= tj < n_lat:
                continue
            ti = (i + d_lon) % n_lon
            pairs.append((i * n_lat + j, ti * n_lat + tj))
    return pairs


def swap_halo(block, axis, count, dim, periodic, w):
    assert count % 2 == 0
    even = lax.rem(lax.axis_index(axis), 2) == 0
    low_side = lax.slice_in_dim(block, 0, w, axis=dim)
    high_side = lax.slice_in_dim(block, block.shape[dim] - w, None, axis=dim)
    inner = [(i, i ^ 1) for i in range(count)]
    outer = [(i, (i + 1) % count if i % 2 else (i - 1) % count) for i in range(count)]
    if not periodic:
        outer = [(i, j) for i, j in outer if abs(i - j) == 1]

    def swap(piece, pairs):
        if dim == block.ndim - 1:
            return lax.ppermute(piece.reshape(-1, 128), axis, pairs).reshape(piece.shape)
        return lax.ppermute(piece, axis, pairs)

    got_inner = swap(jnp.where(even, high_side, low_side), inner)
    got_outer = swap(jnp.where(even, low_side, high_side), outer)
    low = jnp.where(even, got_outer, got_inner)
    high = jnp.where(even, got_inner, got_outer)
    return jnp.concatenate([low, block, high], axis=dim)


def with_halo(fields):
    w = HALO
    n_lon = lax.axis_size("lon")
    n_lat = lax.axis_size("lat")
    flat = [f.reshape((-1,) + f.shape[-2:]) for f in fields]
    planes = [f.shape[0] for f in flat]
    block = jnp.concatenate(flat, axis=0)
    block = swap_halo(block, "lon", n_lon, 1, True, w)
    block = swap_halo(block, "lat", n_lat, 2, False, w)
    out = []
    start = 0
    for f, count in zip(fields, planes):
        out.append(block[start : start + count].reshape(f.shape[:-2] + block.shape[-2:]))
        start += count
    return out


def kernel_term(weight_one, levels, field):
    return weight_one * (
        0.5
        * (1.0 + jax.scipy.special.erf((levels[:, None, None] - field[None, :, :]) * kernel_scale))
    )


def shards(
    height, east, north, depth, coriolis, weight_table, member_index, level_table, threshold_index
):
    local_members, n_x, n_y = height.shape
    w = HALO
    h, e, n, dep, cor = with_halo([height, east, north, depth, coriolis])

    n_lat_total = n_y * lax.axis_size("lat")
    lat0 = lax.axis_index("lat") * n_y - w

    off = 0
    for step in range(ITERS):
        d = dep[off : dep.shape[0] - off, off : dep.shape[1] - off]
        c = cor[off : cor.shape[0] - off, off : cor.shape[1] - off]
        fe = d * e
        fn = d * n
        hn = h[:, 1:-1, 1:-1] - courant_half * (
            (fe[:, 2:, 1:-1] - fe[:, :-2, 1:-1]) + (fn[:, 1:-1, 2:] - fn[:, 1:-1, :-2])
        )
        cols = lat0 + off + 1 + lax.broadcasted_iota(jnp.int32, (1, 1, hn.shape[2]), 2)
        inside = (cols >= 0) & (cols < n_lat_total)
        hn = jnp.where(inside, hn, 0.0)
        en = (
            e[:, 2:-2, 1:-1]
            + c[None, 2:-2, 1:-1] * n[:, 2:-2, 1:-1]
            - courant_half * (hn[:, 2:, :] - hn[:, :-2, :])
        )
        nn = (
            n[:, 2:-2, 2:-2]
            - c[None, 2:-2, 2:-2] * en[:, :, 1:-1]
            - courant_half * (hn[:, 1:-1, 2:] - hn[:, 1:-1, :-2])
        )
        h = hn[:, 1:-1, 1:-1]
        e = en[:, :, 1:-1]
        n = nn
        off += 2
    height = h

    picked = jnp.sum(
        jnp.where(
            member_index[:, None] == jnp.arange(NWEIGHT, dtype=jnp.int32)[None, :],
            weight_table[None, :],
            0.0,
        ),
        axis=1,
    )
    weights = picked / jnp.sum(picked)
    levels = jnp.sum(
        jnp.where(
            threshold_index[:, None] == jnp.arange(NTHR, dtype=jnp.int32)[None, :],
            level_table[None, :],
            0.0,
        ),
        axis=1,
    )
    n_mem = lax.axis_size("mem")
    assert n_mem == 2
    g = lax.axis_index("mem")
    own_rows = NTHR // n_mem
    own_weights = lax.dynamic_slice_in_dim(weights, g * local_members, local_members)
    own_levels = lax.dynamic_slice_in_dim(levels, g * own_rows, own_rows)
    other_levels = lax.dynamic_slice_in_dim(levels, (1 - g) * own_rows, own_rows)

    def partial(lv):
        total = kernel_term(own_weights[0], lv, height[0])
        for member in range(1, local_members):
            total = total + kernel_term(own_weights[member], lv, height[member])
        return total

    sent = lax.ppermute(partial(other_levels), "mem", [(0, 1), (1, 0)])
    mixture_cdf = partial(own_levels) + sent
    return (height, mixture_cdf)


def solution(mesh):
    in_specs = (
        P("mem", "lon", "lat"),
        P("mem", "lon", "lat"),
        P("mem", "lon", "lat"),
        P("lon", "lat"),
        P("lon", "lat"),
        P(),
        P(),
        P(),
        P(),
    )
    out_specs = (P("mem", "lon", "lat"), P("mem", "lon", "lat"))
    return jax.shard_map(shards, mesh=mesh, in_specs=in_specs, out_specs=out_specs, check_vma=False)
```

```python
import jax
import jax.numpy as jnp
from jax import lax
from jax.sharding import PartitionSpec as P
from jax.experimental import pallas as pl

ITERS = 8
NTHR = 16
NWEIGHT = 4

courant_half = 0.45
kernel_scale = 1.0 / (0.5 * 1.4142135623730951)

HALO = 2 * ITERS


def ring_pairs(count, shift, periodic):
    pairs = []
    for i in range(count):
        j = i + shift
        if periodic:
            j %= count
        elif not 0 <= j < count:
            continue
        pairs.append((i, j))
    return pairs


def grid_pairs(n_lon, n_lat, d_lon, d_lat):
    pairs = []
    for i in range(n_lon):
        for j in range(n_lat):
            tj = j + d_lat
            if not 0 <= tj < n_lat:
                continue
            ti = (i + d_lon) % n_lon
            pairs.append((i * n_lat + j, ti * n_lat + tj))
    return pairs


def pack(flat, w):
    planes = [f.shape[0] for f in flat]
    total = sum(planes)
    rows, cols = flat[0].shape[1:]

    def kernel(*refs):
        ins, (block_ref, last_ref, first_ref) = refs[: len(flat)], refs[len(flat) :]
        start = 0
        for ref, count in zip(ins, planes):
            value = ref[...]
            block_ref[start : start + count] = value
            last_ref[start : start + count] = value[:, rows - w :, :]
            first_ref[start : start + count] = value[:, :w, :]
            start += count

    shapes = (
        jax.ShapeDtypeStruct((total, rows, cols), flat[0].dtype),
        jax.ShapeDtypeStruct((total, w, cols), flat[0].dtype),
        jax.ShapeDtypeStruct((total, w, cols), flat[0].dtype),
    )
    return pl.pallas_call(
        kernel,
        out_shape=shapes,
        cost_estimate=pl.CostEstimate(
            flops=0, transcendentals=0, bytes_accessed=8 * total * (rows + w) * cols
        ),
    )(*flat)


def with_halo(fields):
    w = HALO
    n_lon = lax.axis_size("lon")
    n_lat = lax.axis_size("lat")
    flat = [f.reshape((-1,) + f.shape[-2:]) for f in fields]
    planes = [f.shape[0] for f in flat]
    block, last_rows, first_rows = pack(flat, w)
    low = lax.ppermute(last_rows, "lon", ring_pairs(n_lon, 1, True))
    high = lax.ppermute(first_rows, "lon", ring_pairs(n_lon, -1, True))
    block = jnp.concatenate([low, block, high], axis=1)

    def lat_swap(piece, pairs):
        got = lax.ppermute(piece.reshape(-1, 128), "lat", pairs)
        return got.reshape(piece.shape)

    even = lax.rem(lax.axis_index("lat"), 2) == 0
    first_side = jnp.where(even, block[:, :, -w:], block[:, :, :w])
    second_side = jnp.where(even, block[:, :, :w], block[:, :, -w:])
    inner = [(i, i ^ 1) for i in range(n_lat - n_lat % 2)]
    outer = [(i, i + 1 if i % 2 else i - 1) for i in range(1, n_lat - 1)]
    got_first = lat_swap(first_side, inner)
    got_second = lat_swap(second_side, outer)
    low = jnp.where(even, got_second, got_first)
    high = jnp.where(even, got_first, got_second)
    block = jnp.concatenate([low, block, high], axis=2)
    out = []
    start = 0
    for f, count in zip(fields, planes):
        out.append(block[start : start + count].reshape(f.shape[:-2] + block.shape[-2:]))
        start += count
    return out


def kernel_term(weight_one, levels, field):
    return weight_one * (
        0.5
        * (1.0 + jax.scipy.special.erf((levels[:, None, None] - field[None, :, :]) * kernel_scale))
    )


def shards(
    height, east, north, depth, coriolis, weight_table, member_index, level_table, threshold_index
):
    local_members, n_x, n_y = height.shape
    w = HALO
    h, e, n, dep, cor = with_halo([height, east, north, depth, coriolis])

    n_lat_total = n_y * lax.axis_size("lat")
    lat0 = lax.axis_index("lat") * n_y - w

    off = 0
    for step in range(ITERS):
        d = dep[off : dep.shape[0] - off, off : dep.shape[1] - off]
        c = cor[off : cor.shape[0] - off, off : cor.shape[1] - off]
        fe = d * e
        fn = d * n
        hn = h[:, 1:-1, 1:-1] - courant_half * (
            (fe[:, 2:, 1:-1] - fe[:, :-2, 1:-1]) + (fn[:, 1:-1, 2:] - fn[:, 1:-1, :-2])
        )
        cols = lat0 + off + 1 + lax.broadcasted_iota(jnp.int32, (1, 1, hn.shape[2]), 2)
        inside = (cols >= 0) & (cols < n_lat_total)
        hn = jnp.where(inside, hn, 0.0)
        en = (
            e[:, 2:-2, 1:-1]
            + c[None, 2:-2, 1:-1] * n[:, 2:-2, 1:-1]
            - courant_half * (hn[:, 2:, :] - hn[:, :-2, :])
        )
        nn = (
            n[:, 2:-2, 2:-2]
            - c[None, 2:-2, 2:-2] * en[:, :, 1:-1]
            - courant_half * (hn[:, 1:-1, 2:] - hn[:, 1:-1, :-2])
        )
        h = hn[:, 1:-1, 1:-1]
        e = en[:, :, 1:-1]
        n = nn
        off += 2
    height = h

    picked = jnp.sum(
        jnp.where(
            member_index[:, None] == jnp.arange(NWEIGHT, dtype=jnp.int32)[None, :],
            weight_table[None, :],
            0.0,
        ),
        axis=1,
    )
    weights = picked / jnp.sum(picked)
    levels = jnp.sum(
        jnp.where(
            threshold_index[:, None] == jnp.arange(NTHR, dtype=jnp.int32)[None, :],
            level_table[None, :],
            0.0,
        ),
        axis=1,
    )
    n_mem = lax.axis_size("mem")
    assert n_mem == 2
    g = lax.axis_index("mem")
    own_rows = NTHR // n_mem
    own_weights = lax.dynamic_slice_in_dim(weights, g * local_members, local_members)
    own_levels = lax.dynamic_slice_in_dim(levels, g * own_rows, own_rows)
    other_levels = lax.dynamic_slice_in_dim(levels, (1 - g) * own_rows, own_rows)

    def partial(lv):
        total = kernel_term(own_weights[0], lv, height[0])
        for member in range(1, local_members):
            total = total + kernel_term(own_weights[member], lv, height[member])
        return total

    sent = lax.ppermute(partial(other_levels), "mem", [(0, 1), (1, 0)])
    mixture_cdf = partial(own_levels) + sent
    return (height, mixture_cdf)


def solution(mesh):
    in_specs = (
        P("mem", "lon", "lat"),
        P("mem", "lon", "lat"),
        P("mem", "lon", "lat"),
        P("lon", "lat"),
        P("lon", "lat"),
        P(),
        P(),
        P(),
        P(),
    )
    out_specs = (P("mem", "lon", "lat"), P("mem", "lon", "lat"))
    return jax.shard_map(shards, mesh=mesh, in_specs=in_specs, out_specs=out_specs, check_vma=False)
```

```python
import jax
import jax.numpy as jnp
from jax import lax
from jax.sharding import PartitionSpec as P
from jax.experimental import pallas as pl

ITERS = 8
NTHR = 16
NWEIGHT = 4

courant_half = 0.45
kernel_scale = 1.0 / (0.5 * 1.4142135623730951)

HALO = 2 * ITERS


def ring_pairs(count, shift, periodic):
    pairs = []
    for i in range(count):
        j = i + shift
        if periodic:
            j %= count
        elif not 0 <= j < count:
            continue
        pairs.append((i, j))
    return pairs


def grid_pairs(n_lon, n_lat, d_lon, d_lat):
    pairs = []
    for i in range(n_lon):
        for j in range(n_lat):
            tj = j + d_lat
            if not 0 <= tj < n_lat:
                continue
            ti = (i + d_lon) % n_lon
            pairs.append((i * n_lat + j, ti * n_lat + tj))
    return pairs


def edge_rows(flat, w):
    planes = [f.shape[0] for f in flat]
    total = sum(planes)
    rows, cols = flat[0].shape[1:]
    assert rows % w == 0
    n = len(flat)

    def kernel(*refs):
        firsts, lasts = refs[:n], refs[n : 2 * n]
        first_ref, last_ref = refs[2 * n :]
        start = 0
        for f_ref, l_ref, count in zip(firsts, lasts, planes):
            first_ref[start : start + count] = f_ref[...]
            last_ref[start : start + count] = l_ref[...]
            start += count

    def spec(count, block):
        return pl.BlockSpec((count, w, cols), lambda i: (0, block, 0))

    in_specs = [spec(c, 0) for c in planes] + [spec(c, rows // w - 1) for c in planes]
    shape = jax.ShapeDtypeStruct((total, w, cols), flat[0].dtype)
    out_spec = pl.BlockSpec((total, w, cols), lambda i: (0, 0, 0))
    return pl.pallas_call(
        kernel,
        grid=(1,),
        in_specs=in_specs,
        out_specs=(out_spec, out_spec),
        out_shape=(shape, shape),
        cost_estimate=pl.CostEstimate(flops=0, transcendentals=0, bytes_accessed=16 * total * w * cols),
    )(*flat, *flat)


def with_halo(fields):
    w = HALO
    n_lon = lax.axis_size("lon")
    n_lat = lax.axis_size("lat")
    flat = [f.reshape((-1,) + f.shape[-2:]) for f in fields]
    planes = [f.shape[0] for f in flat]
    first_rows, last_rows = edge_rows(flat, w)
    block = jnp.concatenate(flat, axis=0)
    low = lax.ppermute(last_rows, "lon", ring_pairs(n_lon, 1, True))
    high = lax.ppermute(first_rows, "lon", ring_pairs(n_lon, -1, True))
    block = jnp.concatenate([low, block, high], axis=1)

    def lat_swap(piece, pairs):
        got = lax.ppermute(piece.reshape(-1, 128), "lat", pairs)
        return got.reshape(piece.shape)

    even = lax.rem(lax.axis_index("lat"), 2) == 0
    first_side = jnp.where(even, block[:, :, -w:], block[:, :, :w])
    second_side = jnp.where(even, block[:, :, :w], block[:, :, -w:])
    inner = [(i, i ^ 1) for i in range(n_lat - n_lat % 2)]
    outer = [(i, i + 1 if i % 2 else i - 1) for i in range(1, n_lat - 1)]
    got_first = lat_swap(first_side, inner)
    got_second = lat_swap(second_side, outer)
    low = jnp.where(even, got_second, got_first)
    high = jnp.where(even, got_first, got_second)
    block = jnp.concatenate([low, block, high], axis=2)
    out = []
    start = 0
    for f, count in zip(fields, planes):
        out.append(block[start : start + count].reshape(f.shape[:-2] + block.shape[-2:]))
        start += count
    return out


def kernel_term(weight_one, levels, field):
    return weight_one * (
        0.5
        * (1.0 + jax.scipy.special.erf((levels[:, None, None] - field[None, :, :]) * kernel_scale))
    )


def shards(
    height, east, north, depth, coriolis, weight_table, member_index, level_table, threshold_index
):
    local_members, n_x, n_y = height.shape
    w = HALO
    h, e, n, dep, cor = with_halo([height, east, north, depth, coriolis])

    n_lat_total = n_y * lax.axis_size("lat")
    lat0 = lax.axis_index("lat") * n_y - w

    off = 0
    for step in range(ITERS):
        d = dep[off : dep.shape[0] - off, off : dep.shape[1] - off]
        c = cor[off : cor.shape[0] - off, off : cor.shape[1] - off]
        fe = d * e
        fn = d * n
        hn = h[:, 1:-1, 1:-1] - courant_half * (
            (fe[:, 2:, 1:-1] - fe[:, :-2, 1:-1]) + (fn[:, 1:-1, 2:] - fn[:, 1:-1, :-2])
        )
        cols = lat0 + off + 1 + lax.broadcasted_iota(jnp.int32, (1, 1, hn.shape[2]), 2)
        inside = (cols >= 0) & (cols < n_lat_total)
        hn = jnp.where(inside, hn, 0.0)
        en = (
            e[:, 2:-2, 1:-1]
            + c[None, 2:-2, 1:-1] * n[:, 2:-2, 1:-1]
            - courant_half * (hn[:, 2:, :] - hn[:, :-2, :])
        )
        nn = (
            n[:, 2:-2, 2:-2]
            - c[None, 2:-2, 2:-2] * en[:, :, 1:-1]
            - courant_half * (hn[:, 1:-1, 2:] - hn[:, 1:-1, :-2])
        )
        h = hn[:, 1:-1, 1:-1]
        e = en[:, :, 1:-1]
        n = nn
        off += 2
    height = h

    picked = jnp.sum(
        jnp.where(
            member_index[:, None] == jnp.arange(NWEIGHT, dtype=jnp.int32)[None, :],
            weight_table[None, :],
            0.0,
        ),
        axis=1,
    )
    weights = picked / jnp.sum(picked)
    levels = jnp.sum(
        jnp.where(
            threshold_index[:, None] == jnp.arange(NTHR, dtype=jnp.int32)[None, :],
            level_table[None, :],
            0.0,
        ),
        axis=1,
    )
    n_mem = lax.axis_size("mem")
    assert n_mem == 2
    g = lax.axis_index("mem")
    own_rows = NTHR // n_mem
    own_weights = lax.dynamic_slice_in_dim(weights, g * local_members, local_members)
    own_levels = lax.dynamic_slice_in_dim(levels, g * own_rows, own_rows)
    other_levels = lax.dynamic_slice_in_dim(levels, (1 - g) * own_rows, own_rows)

    def partial(lv):
        total = kernel_term(own_weights[0], lv, height[0])
        for member in range(1, local_members):
            total = total + kernel_term(own_weights[member], lv, height[member])
        return total

    sent = lax.ppermute(partial(other_levels), "mem", [(0, 1), (1, 0)])
    mixture_cdf = partial(own_levels) + sent
    return (height, mixture_cdf)


def solution(mesh):
    in_specs = (
        P("mem", "lon", "lat"),
        P("mem", "lon", "lat"),
        P("mem", "lon", "lat"),
        P("lon", "lat"),
        P("lon", "lat"),
        P(),
        P(),
        P(),
        P(),
    )
    out_specs = (P("mem", "lon", "lat"), P("mem", "lon", "lat"))
    return jax.shard_map(shards, mesh=mesh, in_specs=in_specs, out_specs=out_specs, check_vma=False)
```

```python
import jax
import jax.numpy as jnp
from jax import lax
from jax.sharding import PartitionSpec as P
from jax.experimental import pallas as pl

ITERS = 8
NTHR = 16
NWEIGHT = 4

courant_half = 0.45
kernel_scale = 1.0 / (0.5 * 1.4142135623730951)

HALO = 2 * ITERS


def ring_pairs(count, shift, periodic):
    pairs = []
    for i in range(count):
        j = i + shift
        if periodic:
            j %= count
        elif not 0 <= j < count:
            continue
        pairs.append((i, j))
    return pairs


def grid_pairs(n_lon, n_lat, d_lon, d_lat):
    pairs = []
    for i in range(n_lon):
        for j in range(n_lat):
            tj = j + d_lat
            if not 0 <= tj < n_lat:
                continue
            ti = (i + d_lon) % n_lon
            pairs.append((i * n_lat + j, ti * n_lat + tj))
    return pairs


def edge_rows(flat, w):
    planes = [f.shape[0] for f in flat]
    total = sum(planes)
    rows, cols = flat[0].shape[1:]
    assert rows % w == 0
    n = len(flat)

    def kernel(*refs):
        firsts, lasts = refs[:n], refs[n : 2 * n]
        first_ref, last_ref = refs[2 * n :]
        start = 0
        for f_ref, l_ref, count in zip(firsts, lasts, planes):
            first_ref[start : start + count] = f_ref[...]
            last_ref[start : start + count] = l_ref[...]
            start += count

    def spec(count, block):
        return pl.BlockSpec((count, w, cols), lambda i: (0, block, 0))

    in_specs = [spec(c, 0) for c in planes] + [spec(c, rows // w - 1) for c in planes]
    shape = jax.ShapeDtypeStruct((total, w, cols), flat[0].dtype)
    out_spec = pl.BlockSpec((total, w, cols), lambda i: (0, 0, 0))
    return pl.pallas_call(
        kernel,
        grid=(1,),
        in_specs=in_specs,
        out_specs=(out_spec, out_spec),
        out_shape=(shape, shape),
        cost_estimate=pl.CostEstimate(flops=0, transcendentals=0, bytes_accessed=16 * total * w * cols),
    )(*flat, *flat)


def with_halo(fields):
    w = HALO
    n_lon = lax.axis_size("lon")
    n_lat = lax.axis_size("lat")
    flat = [f.reshape((-1,) + f.shape[-2:]) for f in fields]
    planes = [f.shape[0] for f in flat]
    first_rows, last_rows = edge_rows(flat, w)
    block = jnp.concatenate(flat, axis=0)
    low = lax.ppermute(last_rows, "lon", ring_pairs(n_lon, 1, True))
    high = lax.ppermute(first_rows, "lon", ring_pairs(n_lon, -1, True))
    block = jnp.concatenate([low, block, high], axis=1)

    me = lax.axis_index("lat")
    low_side = block[:, :, :w]
    high_side = block[:, :, -w:]
    shape = low_side.shape
    zero = jnp.zeros_like(low_side)
    chunks = jnp.stack(
        [jnp.where(k == me + 1, high_side, jnp.where(k == me - 1, low_side, zero)).reshape(-1, 128)
         for k in range(n_lat)]
    )
    got = lax.all_to_all(chunks, "lat", 0, 0, tiled=False)
    below = lax.dynamic_index_in_dim(got, jnp.maximum(me - 1, 0), 0, keepdims=False).reshape(shape)
    above = lax.dynamic_index_in_dim(got, jnp.minimum(me + 1, n_lat - 1), 0, keepdims=False).reshape(shape)
    low = jnp.where(me > 0, below, zero)
    high = jnp.where(me < n_lat - 1, above, zero)
    block = jnp.concatenate([low, block, high], axis=2)
    out = []
    start = 0
    for f, count in zip(fields, planes):
        out.append(block[start : start + count].reshape(f.shape[:-2] + block.shape[-2:]))
        start += count
    return out


def kernel_term(weight_one, levels, field):
    return weight_one * (
        0.5
        * (1.0 + jax.scipy.special.erf((levels[:, None, None] - field[None, :, :]) * kernel_scale))
    )


def shards(
    height, east, north, depth, coriolis, weight_table, member_index, level_table, threshold_index
):
    local_members, n_x, n_y = height.shape
    w = HALO
    h, e, n, dep, cor = with_halo([height, east, north, depth, coriolis])

    n_lat_total = n_y * lax.axis_size("lat")
    lat0 = lax.axis_index("lat") * n_y - w

    off = 0
    for step in range(ITERS):
        d = dep[off : dep.shape[0] - off, off : dep.shape[1] - off]
        c = cor[off : cor.shape[0] - off, off : cor.shape[1] - off]
        fe = d * e
        fn = d * n
        hn = h[:, 1:-1, 1:-1] - courant_half * (
            (fe[:, 2:, 1:-1] - fe[:, :-2, 1:-1]) + (fn[:, 1:-1, 2:] - fn[:, 1:-1, :-2])
        )
        cols = lat0 + off + 1 + lax.broadcasted_iota(jnp.int32, (1, 1, hn.shape[2]), 2)
        inside = (cols >= 0) & (cols < n_lat_total)
        hn = jnp.where(inside, hn, 0.0)
        en = (
            e[:, 2:-2, 1:-1]
            + c[None, 2:-2, 1:-1] * n[:, 2:-2, 1:-1]
            - courant_half * (hn[:, 2:, :] - hn[:, :-2, :])
        )
        nn = (
            n[:, 2:-2, 2:-2]
            - c[None, 2:-2, 2:-2] * en[:, :, 1:-1]
            - courant_half * (hn[:, 1:-1, 2:] - hn[:, 1:-1, :-2])
        )
        h = hn[:, 1:-1, 1:-1]
        e = en[:, :, 1:-1]
        n = nn
        off += 2
    height = h

    picked = jnp.sum(
        jnp.where(
            member_index[:, None] == jnp.arange(NWEIGHT, dtype=jnp.int32)[None, :],
            weight_table[None, :],
            0.0,
        ),
        axis=1,
    )
    weights = picked / jnp.sum(picked)
    levels = jnp.sum(
        jnp.where(
            threshold_index[:, None] == jnp.arange(NTHR, dtype=jnp.int32)[None, :],
            level_table[None, :],
            0.0,
        ),
        axis=1,
    )
    n_mem = lax.axis_size("mem")
    assert n_mem == 2
    g = lax.axis_index("mem")
    own_rows = NTHR // n_mem
    own_weights = lax.dynamic_slice_in_dim(weights, g * local_members, local_members)
    own_levels = lax.dynamic_slice_in_dim(levels, g * own_rows, own_rows)
    other_levels = lax.dynamic_slice_in_dim(levels, (1 - g) * own_rows, own_rows)

    def partial(lv):
        total = kernel_term(own_weights[0], lv, height[0])
        for member in range(1, local_members):
            total = total + kernel_term(own_weights[member], lv, height[member])
        return total

    sent = lax.ppermute(partial(other_levels), "mem", [(0, 1), (1, 0)])
    mixture_cdf = partial(own_levels) + sent
    return (height, mixture_cdf)


def solution(mesh):
    in_specs = (
        P("mem", "lon", "lat"),
        P("mem", "lon", "lat"),
        P("mem", "lon", "lat"),
        P("lon", "lat"),
        P("lon", "lat"),
        P(),
        P(),
        P(),
        P(),
    )
    out_specs = (P("mem", "lon", "lat"), P("mem", "lon", "lat"))
    return jax.shard_map(shards, mesh=mesh, in_specs=in_specs, out_specs=out_specs, check_vma=False)
```

```python
import jax
import jax.numpy as jnp
from jax import lax
from jax.sharding import PartitionSpec as P
from jax.experimental import pallas as pl

ITERS = 8
NTHR = 16
NWEIGHT = 4

courant_half = 0.45
kernel_scale = 1.0 / (0.5 * 1.4142135623730951)

HALO = 2 * ITERS


def ring_pairs(count, shift, periodic):
    pairs = []
    for i in range(count):
        j = i + shift
        if periodic:
            j %= count
        elif not 0 <= j < count:
            continue
        pairs.append((i, j))
    return pairs


def grid_pairs(n_lon, n_lat, d_lon, d_lat):
    pairs = []
    for i in range(n_lon):
        for j in range(n_lat):
            tj = j + d_lat
            if not 0 <= tj < n_lat:
                continue
            ti = (i + d_lon) % n_lon
            pairs.append((i * n_lat + j, ti * n_lat + tj))
    return pairs


def edge_rows(flat, w):
    planes = [f.shape[0] for f in flat]
    total = sum(planes)
    rows, cols = flat[0].shape[1:]
    assert rows % w == 0
    n = len(flat)

    def kernel(*refs):
        firsts, lasts = refs[:n], refs[n : 2 * n]
        first_ref, last_ref = refs[2 * n :]
        start = 0
        for f_ref, l_ref, count in zip(firsts, lasts, planes):
            first_ref[start : start + count] = f_ref[...]
            last_ref[start : start + count] = l_ref[...]
            start += count

    def spec(count, block):
        return pl.BlockSpec((count, w, cols), lambda i: (0, block, 0))

    in_specs = [spec(c, 0) for c in planes] + [spec(c, rows // w - 1) for c in planes]
    shape = jax.ShapeDtypeStruct((total, w, cols), flat[0].dtype)
    out_spec = pl.BlockSpec((total, w, cols), lambda i: (0, 0, 0))
    return pl.pallas_call(
        kernel,
        grid=(1,),
        in_specs=in_specs,
        out_specs=(out_spec, out_spec),
        out_shape=(shape, shape),
        cost_estimate=pl.CostEstimate(flops=0, transcendentals=0, bytes_accessed=16 * total * w * cols),
    )(*flat, *flat)


def with_halo(fields):
    w = HALO
    n_lon = lax.axis_size("lon")
    n_lat = lax.axis_size("lat")
    flat = [f.reshape((-1,) + f.shape[-2:]) for f in fields]
    planes = [f.shape[0] for f in flat]
    first_rows, last_rows = edge_rows(flat, w)
    block = jnp.concatenate(flat, axis=0)
    low = lax.ppermute(last_rows, "lon", ring_pairs(n_lon, 1, True))
    high = lax.ppermute(first_rows, "lon", ring_pairs(n_lon, -1, True))
    block = jnp.concatenate([low, block, high], axis=1)

    def lat_swap(piece, pairs):
        got = lax.ppermute(piece.reshape(-1, 128), "lat", pairs)
        return got.reshape(piece.shape)

    even = lax.rem(lax.axis_index("lat"), 2) == 0
    first_side = jnp.where(even, block[:, :, -w:], block[:, :, :w])
    second_side = jnp.where(even, block[:, :, :w], block[:, :, -w:])
    inner = [(i, i ^ 1) for i in range(n_lat - n_lat % 2)]
    outer = [(i, i + 1 if i % 2 else i - 1) for i in range(1, n_lat - 1)]
    got_second = lat_swap(second_side, outer)
    got_first = lat_swap(first_side, inner)
    low = jnp.where(even, got_second, got_first)
    high = jnp.where(even, got_first, got_second)
    block = jnp.concatenate([low, block, high], axis=2)
    out = []
    start = 0
    for f, count in zip(fields, planes):
        out.append(block[start : start + count].reshape(f.shape[:-2] + block.shape[-2:]))
        start += count
    return out


def kernel_term(weight_one, levels, field):
    return weight_one * (
        0.5
        * (1.0 + jax.scipy.special.erf((levels[:, None, None] - field[None, :, :]) * kernel_scale))
    )


def shards(
    height, east, north, depth, coriolis, weight_table, member_index, level_table, threshold_index
):
    local_members, n_x, n_y = height.shape
    w = HALO
    h, e, n, dep, cor = with_halo([height, east, north, depth, coriolis])

    n_lat_total = n_y * lax.axis_size("lat")
    lat0 = lax.axis_index("lat") * n_y - w

    off = 0
    for step in range(ITERS):
        d = dep[off : dep.shape[0] - off, off : dep.shape[1] - off]
        c = cor[off : cor.shape[0] - off, off : cor.shape[1] - off]
        fe = d * e
        fn = d * n
        hn = h[:, 1:-1, 1:-1] - courant_half * (
            (fe[:, 2:, 1:-1] - fe[:, :-2, 1:-1]) + (fn[:, 1:-1, 2:] - fn[:, 1:-1, :-2])
        )
        cols = lat0 + off + 1 + lax.broadcasted_iota(jnp.int32, (1, 1, hn.shape[2]), 2)
        inside = (cols >= 0) & (cols < n_lat_total)
        hn = jnp.where(inside, hn, 0.0)
        en = (
            e[:, 2:-2, 1:-1]
            + c[None, 2:-2, 1:-1] * n[:, 2:-2, 1:-1]
            - courant_half * (hn[:, 2:, :] - hn[:, :-2, :])
        )
        nn = (
            n[:, 2:-2, 2:-2]
            - c[None, 2:-2, 2:-2] * en[:, :, 1:-1]
            - courant_half * (hn[:, 1:-1, 2:] - hn[:, 1:-1, :-2])
        )
        h = hn[:, 1:-1, 1:-1]
        e = en[:, :, 1:-1]
        n = nn
        off += 2
    height = h

    picked = jnp.sum(
        jnp.where(
            member_index[:, None] == jnp.arange(NWEIGHT, dtype=jnp.int32)[None, :],
            weight_table[None, :],
            0.0,
        ),
        axis=1,
    )
    weights = picked / jnp.sum(picked)
    levels = jnp.sum(
        jnp.where(
            threshold_index[:, None] == jnp.arange(NTHR, dtype=jnp.int32)[None, :],
            level_table[None, :],
            0.0,
        ),
        axis=1,
    )
    n_mem = lax.axis_size("mem")
    assert n_mem == 2
    g = lax.axis_index("mem")
    own_rows = NTHR // n_mem
    own_weights = lax.dynamic_slice_in_dim(weights, g * local_members, local_members)
    own_levels = lax.dynamic_slice_in_dim(levels, g * own_rows, own_rows)
    other_levels = lax.dynamic_slice_in_dim(levels, (1 - g) * own_rows, own_rows)

    def partial(lv):
        total = kernel_term(own_weights[0], lv, height[0])
        for member in range(1, local_members):
            total = total + kernel_term(own_weights[member], lv, height[member])
        return total

    sent = lax.ppermute(partial(other_levels), "mem", [(0, 1), (1, 0)])
    mixture_cdf = partial(own_levels) + sent
    return (height, mixture_cdf)


def solution(mesh):
    in_specs = (
        P("mem", "lon", "lat"),
        P("mem", "lon", "lat"),
        P("mem", "lon", "lat"),
        P("lon", "lat"),
        P("lon", "lat"),
        P(),
        P(),
        P(),
        P(),
    )
    out_specs = (P("mem", "lon", "lat"), P("mem", "lon", "lat"))
    return jax.shard_map(shards, mesh=mesh, in_specs=in_specs, out_specs=out_specs, check_vma=False)
```

```python
import jax
import jax.numpy as jnp
from jax import lax
from jax.sharding import PartitionSpec as P
from jax.experimental import pallas as pl

ITERS = 8
NTHR = 16
NWEIGHT = 4

courant_half = 0.45
kernel_scale = 1.0 / (0.5 * 1.4142135623730951)

HALO = 2 * ITERS


def ring_pairs(count, shift, periodic):
    pairs = []
    for i in range(count):
        j = i + shift
        if periodic:
            j %= count
        elif not 0 <= j < count:
            continue
        pairs.append((i, j))
    return pairs


def grid_pairs(n_lon, n_lat, d_lon, d_lat):
    pairs = []
    for i in range(n_lon):
        for j in range(n_lat):
            tj = j + d_lat
            if not 0 <= tj < n_lat:
                continue
            ti = (i + d_lon) % n_lon
            pairs.append((i * n_lat + j, ti * n_lat + tj))
    return pairs


def edge_rows(flat, w, block):
    planes = [f.shape[0] for f in flat]
    total = sum(planes)
    rows, cols = flat[0].shape[1:]
    assert rows % w == 0

    def kernel(*refs):
        ins, out_ref = refs[:-1], refs[-1]
        start = 0
        for ref, count in zip(ins, planes):
            out_ref[start : start + count] = ref[...]
            start += count

    in_specs = [pl.BlockSpec((c, w, cols), lambda i: (0, block, 0)) for c in planes]
    return pl.pallas_call(
        kernel,
        grid=(1,),
        in_specs=in_specs,
        out_specs=pl.BlockSpec((total, w, cols), lambda i: (0, 0, 0)),
        out_shape=jax.ShapeDtypeStruct((total, w, cols), flat[0].dtype),
        cost_estimate=pl.CostEstimate(flops=0, transcendentals=0, bytes_accessed=8 * total * w * cols),
    )(*flat)


def with_halo(fields):
    w = HALO
    n_lon = lax.axis_size("lon")
    n_lat = lax.axis_size("lat")
    flat = [f.reshape((-1,) + f.shape[-2:]) for f in fields]
    planes = [f.shape[0] for f in flat]
    rows = flat[0].shape[1]
    low = lax.ppermute(edge_rows(flat, w, rows // w - 1), "lon", ring_pairs(n_lon, 1, True))
    high = lax.ppermute(edge_rows(flat, w, 0), "lon", ring_pairs(n_lon, -1, True))
    block = jnp.concatenate(flat, axis=0)
    block = jnp.concatenate([low, block, high], axis=1)

    def lat_swap(piece, pairs):
        got = lax.ppermute(piece.reshape(-1, 128), "lat", pairs)
        return got.reshape(piece.shape)

    even = lax.rem(lax.axis_index("lat"), 2) == 0
    first_side = jnp.where(even, block[:, :, -w:], block[:, :, :w])
    second_side = jnp.where(even, block[:, :, :w], block[:, :, -w:])
    inner = [(i, i ^ 1) for i in range(n_lat - n_lat % 2)]
    outer = [(i, i + 1 if i % 2 else i - 1) for i in range(1, n_lat - 1)]
    got_first = lat_swap(first_side, inner)
    got_second = lat_swap(second_side, outer)
    low = jnp.where(even, got_second, got_first)
    high = jnp.where(even, got_first, got_second)
    block = jnp.concatenate([low, block, high], axis=2)
    out = []
    start = 0
    for f, count in zip(fields, planes):
        out.append(block[start : start + count].reshape(f.shape[:-2] + block.shape[-2:]))
        start += count
    return out


def kernel_term(weight_one, levels, field):
    return weight_one * (
        0.5
        * (1.0 + jax.scipy.special.erf((levels[:, None, None] - field[None, :, :]) * kernel_scale))
    )


def shards(
    height, east, north, depth, coriolis, weight_table, member_index, level_table, threshold_index
):
    local_members, n_x, n_y = height.shape
    w = HALO
    h, e, n, dep, cor = with_halo([height, east, north, depth, coriolis])

    n_lat_total = n_y * lax.axis_size("lat")
    lat0 = lax.axis_index("lat") * n_y - w

    off = 0
    for step in range(ITERS):
        d = dep[off : dep.shape[0] - off, off : dep.shape[1] - off]
        c = cor[off : cor.shape[0] - off, off : cor.shape[1] - off]
        fe = d * e
        fn = d * n
        hn = h[:, 1:-1, 1:-1] - courant_half * (
            (fe[:, 2:, 1:-1] - fe[:, :-2, 1:-1]) + (fn[:, 1:-1, 2:] - fn[:, 1:-1, :-2])
        )
        cols = lat0 + off + 1 + lax.broadcasted_iota(jnp.int32, (1, 1, hn.shape[2]), 2)
        inside = (cols >= 0) & (cols < n_lat_total)
        hn = jnp.where(inside, hn, 0.0)
        en = (
            e[:, 2:-2, 1:-1]
            + c[None, 2:-2, 1:-1] * n[:, 2:-2, 1:-1]
            - courant_half * (hn[:, 2:, :] - hn[:, :-2, :])
        )
        nn = (
            n[:, 2:-2, 2:-2]
            - c[None, 2:-2, 2:-2] * en[:, :, 1:-1]
            - courant_half * (hn[:, 1:-1, 2:] - hn[:, 1:-1, :-2])
        )
        h = hn[:, 1:-1, 1:-1]
        e = en[:, :, 1:-1]
        n = nn
        off += 2
    height = h

    picked = jnp.sum(
        jnp.where(
            member_index[:, None] == jnp.arange(NWEIGHT, dtype=jnp.int32)[None, :],
            weight_table[None, :],
            0.0,
        ),
        axis=1,
    )
    weights = picked / jnp.sum(picked)
    levels = jnp.sum(
        jnp.where(
            threshold_index[:, None] == jnp.arange(NTHR, dtype=jnp.int32)[None, :],
            level_table[None, :],
            0.0,
        ),
        axis=1,
    )
    n_mem = lax.axis_size("mem")
    assert n_mem == 2
    g = lax.axis_index("mem")
    own_rows = NTHR // n_mem
    own_weights = lax.dynamic_slice_in_dim(weights, g * local_members, local_members)
    own_levels = lax.dynamic_slice_in_dim(levels, g * own_rows, own_rows)
    other_levels = lax.dynamic_slice_in_dim(levels, (1 - g) * own_rows, own_rows)

    def partial(lv):
        total = kernel_term(own_weights[0], lv, height[0])
        for member in range(1, local_members):
            total = total + kernel_term(own_weights[member], lv, height[member])
        return total

    sent = lax.ppermute(partial(other_levels), "mem", [(0, 1), (1, 0)])
    mixture_cdf = partial(own_levels) + sent
    return (height, mixture_cdf)


def solution(mesh):
    in_specs = (
        P("mem", "lon", "lat"),
        P("mem", "lon", "lat"),
        P("mem", "lon", "lat"),
        P("lon", "lat"),
        P("lon", "lat"),
        P(),
        P(),
        P(),
        P(),
    )
    out_specs = (P("mem", "lon", "lat"), P("mem", "lon", "lat"))
    return jax.shard_map(shards, mesh=mesh, in_specs=in_specs, out_specs=out_specs, check_vma=False)
```

```python
import jax
import jax.numpy as jnp
from jax import lax
from jax.sharding import PartitionSpec as P
from jax.experimental import pallas as pl

ITERS = 8
NTHR = 16
NWEIGHT = 4

courant_half = 0.45
kernel_scale = 1.0 / (0.5 * 1.4142135623730951)

HALO = 2 * ITERS


def ring_pairs(count, shift, periodic):
    pairs = []
    for i in range(count):
        j = i + shift
        if periodic:
            j %= count
        elif not 0 <= j < count:
            continue
        pairs.append((i, j))
    return pairs


def grid_pairs(n_lon, n_lat, d_lon, d_lat):
    pairs = []
    for i in range(n_lon):
        for j in range(n_lat):
            tj = j + d_lat
            if not 0 <= tj < n_lat:
                continue
            ti = (i + d_lon) % n_lon
            pairs.append((i * n_lat + j, ti * n_lat + tj))
    return pairs


def edge_rows(flat, w):
    planes = [f.shape[0] for f in flat]
    total = sum(planes)
    rows, cols = flat[0].shape[1:]
    assert rows % w == 0
    n = len(flat)

    def kernel(*refs):
        firsts, lasts = refs[:n], refs[n : 2 * n]
        first_ref, last_ref = refs[2 * n :]
        start = 0
        for f_ref, l_ref, count in zip(firsts, lasts, planes):
            first_ref[start : start + count] = f_ref[...]
            last_ref[start : start + count] = l_ref[...]
            start += count

    def spec(count, block):
        return pl.BlockSpec((count, w, cols), lambda i: (0, block, 0))

    in_specs = [spec(c, 0) for c in planes] + [spec(c, rows // w - 1) for c in planes]
    shape = jax.ShapeDtypeStruct((total, w, cols), flat[0].dtype)
    out_spec = pl.BlockSpec((total, w, cols), lambda i: (0, 0, 0))
    return pl.pallas_call(
        kernel,
        grid=(1,),
        in_specs=in_specs,
        out_specs=(out_spec, out_spec),
        out_shape=(shape, shape),
        cost_estimate=pl.CostEstimate(flops=0, transcendentals=0, bytes_accessed=16 * total * w * cols),
    )(*flat, *flat)


def with_halo(fields):
    w = HALO
    n_lon = lax.axis_size("lon")
    n_lat = lax.axis_size("lat")
    flat = [f.reshape((-1,) + f.shape[-2:]) for f in fields]
    planes = [f.shape[0] for f in flat]
    first_rows, last_rows = edge_rows(flat, w)
    block = jnp.concatenate(flat, axis=0)
    low = lax.ppermute(last_rows, "lon", ring_pairs(n_lon, 1, True))
    high = lax.ppermute(first_rows, "lon", ring_pairs(n_lon, -1, True))
    block = jnp.concatenate([low, block, high], axis=1)

    def lat_swap(piece, pairs):
        got = lax.ppermute(piece.reshape(-1, 128), "lat", pairs)
        return got.reshape(piece.shape)

    even = lax.rem(lax.axis_index("lat"), 2) == 0
    first_side = jnp.where(even, block[:, :, -w:], block[:, :, :w])
    second_side = jnp.where(even, block[:, :, :w], block[:, :, -w:])
    inner = [(i, i ^ 1) for i in range(n_lat - n_lat % 2)]
    outer = [(i, i + 1 if i % 2 else i - 1) for i in range(1, n_lat - 1)]
    got_first = lat_swap(first_side, inner)
    got_second = lat_swap(second_side, outer)
    low = jnp.where(even, got_second, got_first)
    high = jnp.where(even, got_first, got_second)
    block = jnp.concatenate([low, block, high], axis=2)
    out = []
    start = 0
    for f, count in zip(fields, planes):
        out.append(block[start : start + count].reshape(f.shape[:-2] + block.shape[-2:]))
        start += count
    return out


def kernel_term(weight_one, levels, field):
    return weight_one * (
        0.5
        * (1.0 + jax.scipy.special.erf((levels[:, None, None] - field[None, :, :]) * kernel_scale))
    )


def shards(
    height, east, north, depth, coriolis, weight_table, member_index, level_table, threshold_index
):
    local_members, n_x, n_y = height.shape
    w = HALO
    h, e, n, dep, cor = with_halo([height, east, north, depth, coriolis])

    n_lat_total = n_y * lax.axis_size("lat")
    lat0 = lax.axis_index("lat") * n_y - w

    off = 0
    for step in range(ITERS):
        d = dep[off : dep.shape[0] - off, off : dep.shape[1] - off]
        c = cor[off : cor.shape[0] - off, off : cor.shape[1] - off]
        fe = d * e
        fn = d * n
        hn = h[:, 1:-1, 1:-1] - courant_half * (
            (fe[:, 2:, 1:-1] - fe[:, :-2, 1:-1]) + (fn[:, 1:-1, 2:] - fn[:, 1:-1, :-2])
        )
        cols = lat0 + off + 1 + lax.broadcasted_iota(jnp.int32, (1, 1, hn.shape[2]), 2)
        inside = (cols >= 0) & (cols < n_lat_total)
        hn = jnp.where(inside, hn, 0.0)
        en = (
            e[:, 2:-2, 1:-1]
            + c[None, 2:-2, 1:-1] * n[:, 2:-2, 1:-1]
            - courant_half * (hn[:, 2:, :] - hn[:, :-2, :])
        )
        nn = (
            n[:, 2:-2, 2:-2]
            - c[None, 2:-2, 2:-2] * en[:, :, 1:-1]
            - courant_half * (hn[:, 1:-1, 2:] - hn[:, 1:-1, :-2])
        )
        h = hn[:, 1:-1, 1:-1]
        e = en[:, :, 1:-1]
        n = nn
        off += 2
    height = h

    picked = jnp.sum(
        jnp.where(
            member_index[:, None] == jnp.arange(NWEIGHT, dtype=jnp.int32)[None, :],
            weight_table[None, :],
            0.0,
        ),
        axis=1,
    )
    weights = picked / jnp.sum(picked)
    levels = jnp.sum(
        jnp.where(
            threshold_index[:, None] == jnp.arange(NTHR, dtype=jnp.int32)[None, :],
            level_table[None, :],
            0.0,
        ),
        axis=1,
    )
    n_mem = lax.axis_size("mem")
    assert n_mem == 2
    g = lax.axis_index("mem")
    own_rows = NTHR // n_mem
    own_weights = lax.dynamic_slice_in_dim(weights, g * local_members, local_members)
    own_levels = lax.dynamic_slice_in_dim(levels, g * own_rows, own_rows)
    other_levels = lax.dynamic_slice_in_dim(levels, (1 - g) * own_rows, own_rows)

    def partial(lv):
        total = kernel_term(own_weights[0], lv, height[0])
        for member in range(1, local_members):
            total = total + kernel_term(own_weights[member], lv, height[member])
        return total

    own, other = lax.optimization_barrier((partial(own_levels), partial(other_levels)))
    sent = lax.ppermute(other, "mem", [(0, 1), (1, 0)])
    mixture_cdf = own + sent
    return (height, mixture_cdf)


def solution(mesh):
    in_specs = (
        P("mem", "lon", "lat"),
        P("mem", "lon", "lat"),
        P("mem", "lon", "lat"),
        P("lon", "lat"),
        P("lon", "lat"),
        P(),
        P(),
        P(),
        P(),
    )
    out_specs = (P("mem", "lon", "lat"), P("mem", "lon", "lat"))
    return jax.shard_map(shards, mesh=mesh, in_specs=in_specs, out_specs=out_specs, check_vma=False)
```
